128 devices in a mesh: node: 4 (over z), local: 32 (over x, y, core).
Axes of the slice: x: 4, y: 4, z: 4, core: 2. Of those that a mesh axis runs over, the one named last changes fastest.
Arguments:
- tokens: bfloat16 [16384, 3584], P(('node', 'local')), may hold values from -6 to 6
- group_ids: int32 [16384, 2], P(('node', 'local')), may hold values from 0 to 3, as said below
- local_ids: int32 [16384, 8], P(('node', 'local')), may hold values from 0 to 31, as said below
- router: bfloat16 [3584, 128], replicated, may hold values from -0.09375 to 0.09375
- w_gate: bfloat16 [128, 3584, 1024], P(('node', 'local')), may hold values from -0.09375 to 0.09375
- w_up: bfloat16 [128, 3584, 1024], P(('node', 'local')), may hold values from -0.09375 to 0.09375
- w_down: bfloat16 [128, 1024, 3584], P(('node', 'local')), may hold values from -0.1875 to 0.1875
Outputs:
- moe_out: bfloat16 [16384, 3584], P(('node', 'local'))
The draws below stay inside these ranges and needn't reach their ends.
Inputs may be any that keep to these rules, and one draw needn't show every extreme that they name: `group_ids`: each token names two different node groups; the tokens of one device name every node group exactly 64 times. `local_ids`: entry k names an expert of node group group_ids[t, k // 4]; the four entries of one group are different. The tokens of one device route at most 10 tokens to one expert, and in every node group some expert receives exactly 10 tokens from every device.
All inputs are finite; a program needn't handle non-finite values.
Results may differ from the reference program's by a relative error of at most 0.0058.
Values may be sent and summed in bfloat16 or wider, within the bound.
No kernel may reach another device: no remote copies, remote signals or barrier semaphores. Data moves between devices by JAX's collectives and lax.ppermute only.
A program may use at most 128 MiB of HBM per device.

```python
import jax
import jax.numpy as jnp
from jax import lax

D = 3584
FF = 1024
TOK_DEV = 128
TOKENS = 16384
EXPERTS = 128
GROUP_EXP = 32
CAP = 10
N_NODE = 4
N_LOCAL = 32


def route_tables(key):
    base_key = jax.random.fold_in(key, 7)
    hot_expert = jax.random.randint(jax.random.fold_in(base_key, 1), (N_NODE,), 0, GROUP_EXP)
    pick_steps = jnp.arange(4, dtype=jnp.int32)
    node_range = jnp.arange(N_NODE, dtype=jnp.int32)

    def one_block(block_index):
        block_key = jax.random.fold_in(base_key, block_index + 2)
        key_rank, key_offset, key_shuffle = jax.random.split(block_key, 3)
        token_rank = jax.random.permutation(key_rank, TOK_DEV).astype(jnp.int32)
        first_group = token_rank % N_NODE
        second_group = (first_group + 1 + token_rank // N_NODE % (N_NODE - 1)) % N_NODE
        groups = jnp.stack([first_group, second_group], axis=1)
        member = ((first_group[:, None] == node_range[None, :]) | (second_group[:, None] == node_range[None, :])).astype(jnp.int32)
        by_rank = jnp.argsort(token_rank)
        sorted_member = member[by_rank]
        earlier = jnp.cumsum(sorted_member, axis=0) - sorted_member
        list_place = earlier[token_rank]
        position = jnp.take_along_axis(list_place, groups, axis=1)
        offset = jax.random.randint(key_offset, (N_NODE,), 0, GROUP_EXP - 1)
        hot_tok = hot_expert[groups]
        capped = jnp.minimum(position, CAP)
        start_at = 3 * capped + 4 * (position - capped) + offset[groups]
        has_hot = position < CAP
        step_shift = jnp.where(has_hot[:, :, None], pick_steps[None, None, :] - 1, pick_steps[None, None, :])
        cycle_index = (start_at[:, :, None] + step_shift) % (GROUP_EXP - 1)
        drawn_pick = cycle_index + (cycle_index >= hot_tok[:, :, None]).astype(jnp.int32)
        group_picks = jnp.where(has_hot[:, :, None] & (pick_steps == 0)[None, None, :], hot_tok[:, :, None], drawn_pick)
        scores = jax.random.randint(key_shuffle, (TOK_DEV, 2, 4), 0, 1 << 20) * 4 + pick_steps[None, None, :]
        shuffle = jnp.argsort(scores, axis=2)
        group_picks = jnp.take_along_axis(group_picks, shuffle, axis=2)
        return (groups, group_picks.reshape(TOK_DEV, 8))
    groups, local_picks = jax.vmap(one_block)(jnp.arange(TOKENS // TOK_DEV, dtype=jnp.int32))
    return (groups.reshape(TOKENS, 2).astype(jnp.int32), local_picks.reshape(TOKENS, 8).astype(jnp.int32))


def draw_group_ids(key, part):
    return route_tables(key)[0]


def draw_local_ids(key, part):
    return route_tables(key)[1]


def levels(own_key, extent, pieces, least, high):
    level = 1.0
    for dim, parts in pieces:
        steps = jax.random.uniform(jax.random.fold_in(jax.random.fold_in(own_key, 6), dim), (parts,), jnp.float32, least / len(pieces), high / len(pieces))
        level = level * jnp.repeat(jnp.exp(steps), extent[dim] // parts).reshape((-1,) + (1,) * (len(extent) - 1 - dim))
    return level


def scatter_about(stream_key, shape, spread, limit, cuts=(), kind=jnp.bfloat16):
    factor_of = levels(stream_key, shape, cuts, -0.22, 0.18) if cuts else 1.0
    array = jax.random.normal(stream_key, shape, jnp.float32) * spread * factor_of
    return jnp.minimum(jnp.maximum(array, -limit), limit).astype(kind)


def setup_inputs(seed: int = 0) -> dict:
    keys = jax.random.split(jax.random.key(seed), 8)
    return {
        "tokens": scatter_about(keys[0], (TOKENS, D), 1.0, 6.0, ((0, 128),)),
        "group_ids": draw_group_ids(jax.random.fold_in(keys[7], 71), 0),
        "local_ids": draw_local_ids(jax.random.fold_in(keys[7], 71), 0),
        "router": scatter_about(keys[3], (D, EXPERTS), D ** -0.5, 0.09375),
        "w_gate": scatter_about(keys[4], (EXPERTS, D, FF), D ** -0.5, 0.09375, ((0, 128),)),
        "w_up": scatter_about(keys[5], (EXPERTS, D, FF), D ** -0.5, 0.09375, ((0, 128),)),
        "w_down": scatter_about(keys[6], (EXPERTS, FF, D), FF ** -0.5, 0.1875, ((0, 128),)),
    }


def reference(tokens, group_ids, local_ids, router, w_gate, w_up, w_down):
    per_group = local_ids.shape[1] // group_ids.shape[1]
    picks_all = local_ids.shape[1]
    expert_ids = (jnp.repeat(group_ids, per_group, axis=1) * GROUP_EXP + local_ids).astype(jnp.int32)
    affinity = jax.nn.sigmoid(jnp.dot(tokens, router, preferred_element_type=jnp.float32))
    picked = jnp.take_along_axis(affinity, expert_ids, axis=1)
    weights = 2.5 * picked / jnp.sum(picked, axis=1, keepdims=True)
    flat_ids = expert_ids.reshape(-1)
    flat_weights = weights.reshape(-1)
    most_rows = N_NODE * N_LOCAL * CAP

    def visit_expert(running_sum, inputs):
        expert, gate_mat, up_mat, down_mat = inputs
        routed_mask = flat_ids == expert
        found_at = jnp.nonzero(routed_mask, size=most_rows, fill_value=0)[0].astype(jnp.int32)
        is_valid = jnp.arange(most_rows, dtype=jnp.int32) < jnp.sum(routed_mask.astype(jnp.int32))
        token_index = (found_at // picks_all).astype(jnp.int32)
        picked_rows = tokens[token_index]
        gate_part = jnp.dot(picked_rows, gate_mat, preferred_element_type=jnp.float32)
        up_part = jnp.dot(picked_rows, up_mat, preferred_element_type=jnp.float32)
        hidden = (jax.nn.silu(gate_part) * up_part).astype(jnp.bfloat16)
        expert_out = jnp.dot(hidden, down_mat, preferred_element_type=jnp.float32).astype(jnp.bfloat16)
        row_scale = jnp.where(is_valid, flat_weights[found_at], jnp.zeros((), flat_weights.dtype))
        running_sum = running_sum.at[token_index].add(row_scale[:, None] * expert_out.astype(running_sum.dtype))
        return running_sum, None

    start_sum = jnp.zeros((tokens.shape[0], tokens.shape[1]), jnp.float32)
    running_sum, _ = lax.scan(visit_expert, start_sum, (jnp.arange(EXPERTS, dtype=jnp.int32), w_gate, w_up, w_down))
    return running_sum.astype(jnp.bfloat16)
```

```python
import jax
import jax.numpy as jnp
from jax import lax
from jax.sharding import PartitionSpec as P

LANES = 128


def slot_positions(targets, bins):
    onehot = (targets[:, None] == jnp.arange(bins, dtype=jnp.int32)[None, :]).astype(jnp.int32)
    earlier = jnp.cumsum(onehot, axis=0) - onehot
    return jnp.sum(earlier * onehot, axis=1)


def fill_slots(source_rows, owners, slot_index, slot_total):
    src_table = jnp.full((slot_total,), source_rows.shape[0], jnp.int32).at[slot_index].set(owners)
    padded = jnp.concatenate(
        [source_rows, jnp.zeros((1, source_rows.shape[1]), source_rows.dtype)], axis=0
    )
    return padded[src_table]


def expert_rows(flat_rows, w_gate, w_up, w_down):
    gate_part = jnp.dot(flat_rows, w_gate[0], preferred_element_type=jnp.float32)
    up_part = jnp.dot(flat_rows, w_up[0], preferred_element_type=jnp.float32)
    hidden = (jax.nn.silu(gate_part) * up_part).astype(jnp.bfloat16)
    return jnp.dot(hidden, w_down[0], preferred_element_type=jnp.float32).astype(jnp.bfloat16)


def on_device(tokens, group_ids, local_ids, router, w_gate, w_up, w_down):
    tok_dev, feat_width = tokens.shape
    node_size = lax.axis_size("node")
    local_size = lax.axis_size("local")
    experts_all = node_size * local_size
    cap_rows = 5 * tok_dev // (2 * local_size)
    group_count = group_ids.shape[1]
    per_group = local_ids.shape[1] // group_count
    expert_ids = jnp.repeat(group_ids, per_group, axis=1) * local_size + local_ids
    affinity = jax.nn.sigmoid(jnp.dot(tokens, router, preferred_element_type=jnp.float32))
    picked = jnp.take_along_axis(affinity, expert_ids, axis=1)
    picked_total = jnp.sum(picked, axis=1)
    flat_ids = expert_ids.reshape(-1)
    slot_index = flat_ids * cap_rows + slot_positions(flat_ids, experts_all)
    owners = jnp.arange(flat_ids.shape[0], dtype=jnp.int32) // local_ids.shape[1]
    wire = (experts_all, cap_rows * feat_width // LANES, LANES)
    send_rows = fill_slots(tokens, owners, slot_index, experts_all * cap_rows).reshape(wire)
    received = lax.all_to_all(send_rows, ("node", "local"), split_axis=0, concat_axis=0, tiled=True)
    produced = expert_rows(received.reshape(-1, feat_width), w_gate, w_up, w_down).reshape(wire)
    returned = lax.all_to_all(produced, ("node", "local"), split_axis=0, concat_axis=0, tiled=True)
    expert_terms = returned.reshape(-1, feat_width)[slot_index].reshape(tok_dev, -1, feat_width)
    weights = 2.5 * picked / picked_total[:, None]
    mixed = jnp.sum(weights[:, :, None] * expert_terms.astype(jnp.float32), axis=1)
    return mixed.astype(jnp.bfloat16)


def solution(mesh):
    return jax.shard_map(
        on_device,
        mesh=mesh,
        in_specs=(
            P(("node", "local"), None),
            P(("node", "local"), None),
            P(("node", "local"), None),
            P(),
            P(("node", "local"), None, None),
            P(("node", "local"), None, None),
            P(("node", "local"), None, None),
        ),
        out_specs=P(("node", "local"), None),
        check_vma=False,
    )
```

```python
import jax
import jax.numpy as jnp
from jax import lax
from jax.sharding import PartitionSpec as P

LANES = 128


def slot_positions(targets, bins):
    onehot = (targets[:, None] == jnp.arange(bins, dtype=jnp.int32)[None, :]).astype(jnp.int32)
    earlier = jnp.cumsum(onehot, axis=0) - onehot
    return jnp.sum(earlier * onehot, axis=1)


def slot_pieces(cap_rows, feat_width):
    tile_rows = 8 * LANES // feat_width if feat_width < 8 * LANES else 1
    whole = [p for p in range(1, cap_rows) if (p * feat_width // LANES) % 8 == 0 and ((cap_rows - p) * feat_width // LANES) % 8 == 0]
    if not whole or cap_rows * feat_width % LANES:
        return (cap_rows,)
    first = min(whole, key=lambda p: abs(2 * p - cap_rows) + (p < cap_rows - p))
    return (first, cap_rows - first)


def expert_rows(flat_rows, w_gate, w_up, w_down):
    gate_part = jnp.dot(flat_rows, w_gate[0], preferred_element_type=jnp.float32)
    up_part = jnp.dot(flat_rows, w_up[0], preferred_element_type=jnp.float32)
    hidden = (jax.nn.silu(gate_part) * up_part).astype(jnp.bfloat16)
    return jnp.dot(hidden, w_down[0], preferred_element_type=jnp.float32).astype(jnp.bfloat16)


def on_device(tokens, group_ids, local_ids, router, w_gate, w_up, w_down):
    tok_dev, feat_width = tokens.shape
    node_size = lax.axis_size("node")
    local_size = lax.axis_size("local")
    experts_all = node_size * local_size
    cap_rows = 5 * tok_dev // (2 * local_size)
    group_count = group_ids.shape[1]
    per_group = local_ids.shape[1] // group_count
    expert_ids = jnp.repeat(group_ids, per_group, axis=1) * local_size + local_ids
    affinity = jax.nn.sigmoid(jnp.dot(tokens, router, preferred_element_type=jnp.float32))
    picked = jnp.take_along_axis(affinity, expert_ids, axis=1)
    picked_total = jnp.sum(picked, axis=1)
    flat_ids = expert_ids.reshape(-1)
    positions = slot_positions(flat_ids, experts_all)
    owners = jnp.arange(flat_ids.shape[0], dtype=jnp.int32) // local_ids.shape[1]
    src_table = jnp.full((experts_all, cap_rows), tok_dev, jnp.int32).at[flat_ids, positions].set(owners)
    padded = jnp.concatenate([tokens, jnp.zeros((1, feat_width), tokens.dtype)], axis=0)
    pieces = slot_pieces(cap_rows, feat_width)
    returned_parts = []
    slot_index = jnp.zeros_like(flat_ids)
    start, base = 0, 0
    for size in pieces:
        wire = (experts_all, size * feat_width // LANES, LANES)
        send_rows = padded[src_table[:, start:start + size].reshape(-1)].reshape(wire)
        received = lax.all_to_all(send_rows, ("node", "local"), split_axis=0, concat_axis=0, tiled=True)
        produced = expert_rows(received.reshape(-1, feat_width), w_gate, w_up, w_down).reshape(wire)
        returned = lax.all_to_all(produced, ("node", "local"), split_axis=0, concat_axis=0, tiled=True)
        returned_parts.append(returned.reshape(-1, feat_width))
        inside = (positions >= start) & (positions < start + size)
        slot_index = jnp.where(inside, base + flat_ids * size + positions - start, slot_index)
        start += size
        base += experts_all * size
    returned = jnp.concatenate(returned_parts, axis=0)
    expert_terms = returned[slot_index].reshape(tok_dev, -1, feat_width)
    weights = 2.5 * picked / picked_total[:, None]
    mixed = jnp.sum(weights[:, :, None] * expert_terms.astype(jnp.float32), axis=1)
    return mixed.astype(jnp.bfloat16)


def solution(mesh):
    return jax.shard_map(
        on_device,
        mesh=mesh,
        in_specs=(
            P(("node", "local"), None),
            P(("node", "local"), None),
            P(("node", "local"), None),
            P(),
            P(("node", "local"), None, None),
            P(("node", "local"), None, None),
            P(("node", "local"), None, None),
        ),
        out_specs=P(("node", "local"), None),
        check_vma=False,
    )
```

```python
import jax
import jax.numpy as jnp
from jax import lax
from jax.sharding import PartitionSpec as P

LANES = 128


def slot_positions(targets, bins):
    onehot = (targets[:, None] == jnp.arange(bins, dtype=jnp.int32)[None, :]).astype(jnp.int32)
    earlier = jnp.cumsum(onehot, axis=0) - onehot
    return jnp.sum(earlier * onehot, axis=1)


def slot_pieces(cap_rows, feat_width):
    tile_rows = 8 * LANES // feat_width if feat_width < 8 * LANES else 1
    whole = [p for p in range(1, cap_rows) if (p * feat_width // LANES) % 8 == 0 and ((cap_rows - p) * feat_width // LANES) % 8 == 0]
    if not whole or cap_rows * feat_width % LANES:
        return (cap_rows,)
    first = min(whole, key=lambda p: abs(2 * p - cap_rows) + (p < cap_rows - p))
    return (first, cap_rows - first)


def combine_piece(rows, weights, flat_ids, positions, start, size):
    tok_dev, picks = weights.shape
    inside = ((positions >= start) & (positions < start + size)).reshape(tok_dev, picks)
    slot = (flat_ids * size + positions - start).reshape(tok_dev, picks)
    hits = slot[:, :, None] == jnp.arange(rows.shape[0], dtype=jnp.int32)[None, None, :]
    dense = jnp.sum(jnp.where(hits & inside[:, :, None], weights[:, :, None], 0.0), axis=1)
    high = dense.astype(jnp.bfloat16)
    low = (dense - high.astype(jnp.float32)).astype(jnp.bfloat16)
    return jnp.dot(high, rows, preferred_element_type=jnp.float32) + jnp.dot(
        low, rows, preferred_element_type=jnp.float32
    )


def expert_rows(flat_rows, w_gate, w_up, w_down):
    gate_part = jnp.dot(flat_rows, w_gate[0], preferred_element_type=jnp.float32)
    up_part = jnp.dot(flat_rows, w_up[0], preferred_element_type=jnp.float32)
    hidden = (jax.nn.silu(gate_part) * up_part).astype(jnp.bfloat16)
    return jnp.dot(hidden, w_down[0], preferred_element_type=jnp.float32).astype(jnp.bfloat16)


def on_device(tokens, group_ids, local_ids, router, w_gate, w_up, w_down):
    tok_dev, feat_width = tokens.shape
    node_size = lax.axis_size("node")
    local_size = lax.axis_size("local")
    experts_all = node_size * local_size
    cap_rows = 5 * tok_dev // (2 * local_size)
    group_count = group_ids.shape[1]
    per_group = local_ids.shape[1] // group_count
    expert_ids = jnp.repeat(group_ids, per_group, axis=1) * local_size + local_ids
    affinity = jax.nn.sigmoid(jnp.dot(tokens, router, preferred_element_type=jnp.float32))
    picked = jnp.take_along_axis(affinity, expert_ids, axis=1)
    picked_total = jnp.sum(picked, axis=1)
    flat_ids = expert_ids.reshape(-1)
    positions = slot_positions(flat_ids, experts_all)
    owners = jnp.arange(flat_ids.shape[0], dtype=jnp.int32) // local_ids.shape[1]
    src_table = jnp.full((experts_all, cap_rows), tok_dev, jnp.int32).at[flat_ids, positions].set(owners)
    padded = jnp.concatenate([tokens, jnp.zeros((1, feat_width), tokens.dtype)], axis=0)
    pieces = slot_pieces(cap_rows, feat_width)
    weights = 2.5 * picked / picked_total[:, None]
    mixed = jnp.zeros((tok_dev, feat_width), jnp.float32)
    start = 0
    for size in pieces:
        wire = (experts_all, size * feat_width // LANES, LANES)
        send_rows = padded[src_table[:, start:start + size].reshape(-1)].reshape(wire)
        received = lax.all_to_all(send_rows, ("node", "local"), split_axis=0, concat_axis=0, tiled=True)
        produced = expert_rows(received.reshape(-1, feat_width), w_gate, w_up, w_down).reshape(wire)
        returned = lax.all_to_all(produced, ("node", "local"), split_axis=0, concat_axis=0, tiled=True)
        mixed = mixed + combine_piece(returned.reshape(-1, feat_width), weights, flat_ids, positions, start, size)
        start += size
    return mixed.astype(jnp.bfloat16)


def solution(mesh):
    return jax.shard_map(
        on_device,
        mesh=mesh,
        in_specs=(
            P(("node", "local"), None),
            P(("node", "local"), None),
            P(("node", "local"), None),
            P(),
            P(("node", "local"), None, None),
            P(("node", "local"), None, None),
            P(("node", "local"), None, None),
        ),
        out_specs=P(("node", "local"), None),
        check_vma=False,
    )
```

```python
import jax
import jax.numpy as jnp
from jax import lax
from jax.sharding import PartitionSpec as P

LANES = 128


def slot_positions(targets, bins):
    onehot = (targets[:, None] == jnp.arange(bins, dtype=jnp.int32)[None, :]).astype(jnp.int32)
    earlier = jnp.cumsum(onehot, axis=0) - onehot
    return jnp.sum(earlier * onehot, axis=1)


def slot_pieces(cap_rows, feat_width):
    tile_rows = 8 * LANES // feat_width if feat_width < 8 * LANES else 1
    whole = [p for p in range(1, cap_rows) if (p * feat_width // LANES) % 8 == 0 and ((cap_rows - p) * feat_width // LANES) % 8 == 0]
    if not whole or cap_rows * feat_width % LANES:
        return (cap_rows,)
    first = min(whole, key=lambda p: abs(2 * p - cap_rows) + (p < cap_rows - p))
    return (first, cap_rows - first)


def gather_piece(tokens, flat_ids, positions, start, size, experts_all):
    tok_dev = tokens.shape[0]
    inside = (positions >= start) & (positions < start + size)
    slot = jnp.where(inside, flat_ids * size + positions - start, -1).reshape(tok_dev, -1)
    hits = slot[None, :, :] == jnp.arange(experts_all * size, dtype=jnp.int32)[:, None, None]
    onehot = jnp.any(hits, axis=2).astype(tokens.dtype)
    return jnp.dot(onehot, tokens, preferred_element_type=jnp.float32).astype(tokens.dtype)


def combine_piece(rows, weights, flat_ids, positions, start, size):
    tok_dev, picks = weights.shape
    inside = ((positions >= start) & (positions < start + size)).reshape(tok_dev, picks)
    slot = (flat_ids * size + positions - start).reshape(tok_dev, picks)
    hits = slot[:, :, None] == jnp.arange(rows.shape[0], dtype=jnp.int32)[None, None, :]
    dense = jnp.sum(jnp.where(hits & inside[:, :, None], weights[:, :, None], 0.0), axis=1)
    high_part = lax.reduce_precision(dense, exponent_bits=8, mantissa_bits=7)
    high = high_part.astype(jnp.bfloat16)
    low = (dense - high_part).astype(jnp.bfloat16)
    return jnp.dot(high, rows, preferred_element_type=jnp.float32) + jnp.dot(
        low, rows, preferred_element_type=jnp.float32
    )


def expert_rows(flat_rows, w_gate, w_up, w_down):
    gate_part = jnp.dot(flat_rows, w_gate[0], preferred_element_type=jnp.float32)
    up_part = jnp.dot(flat_rows, w_up[0], preferred_element_type=jnp.float32)
    hidden = (jax.nn.silu(gate_part) * up_part).astype(jnp.bfloat16)
    return jnp.dot(hidden, w_down[0], preferred_element_type=jnp.float32).astype(jnp.bfloat16)


def on_device(tokens, group_ids, local_ids, router, w_gate, w_up, w_down):
    tok_dev, feat_width = tokens.shape
    node_size = lax.axis_size("node")
    local_size = lax.axis_size("local")
    experts_all = node_size * local_size
    cap_rows = 5 * tok_dev // (2 * local_size)
    group_count = group_ids.shape[1]
    per_group = local_ids.shape[1] // group_count
    expert_ids = jnp.repeat(group_ids, per_group, axis=1) * local_size + local_ids
    affinity = jax.nn.sigmoid(jnp.dot(tokens, router, preferred_element_type=jnp.float32))
    picked = jnp.take_along_axis(affinity, expert_ids, axis=1)
    picked_total = jnp.sum(picked, axis=1)
    flat_ids = expert_ids.reshape(-1)
    positions = slot_positions(flat_ids, experts_all)
    pieces = slot_pieces(cap_rows, feat_width)
    weights = 2.5 * picked / picked_total[:, None]
    mixed = jnp.zeros((tok_dev, feat_width), jnp.float32)
    start = 0
    for size in pieces:
        wire = (experts_all, size * feat_width // LANES, LANES)
        send_rows = gather_piece(tokens, flat_ids, positions, start, size, experts_all).reshape(wire)
        received = lax.all_to_all(send_rows, ("node", "local"), split_axis=0, concat_axis=0, tiled=True)
        produced = expert_rows(received.reshape(-1, feat_width), w_gate, w_up, w_down).reshape(wire)
        returned = lax.all_to_all(produced, ("node", "local"), split_axis=0, concat_axis=0, tiled=True)
        mixed = mixed + combine_piece(returned.reshape(-1, feat_width), weights, flat_ids, positions, start, size)
        start += size
    return mixed.astype(jnp.bfloat16)


def solution(mesh):
    return jax.shard_map(
        on_device,
        mesh=mesh,
        in_specs=(
            P(("node", "local"), None),
            P(("node", "local"), None),
            P(("node", "local"), None),
            P(),
            P(("node", "local"), None, None),
            P(("node", "local"), None, None),
            P(("node", "local"), None, None),
        ),
        out_specs=P(("node", "local"), None),
        check_vma=False,
    )
```

```python
import jax
import jax.numpy as jnp
from jax import lax
from jax.sharding import PartitionSpec as P

LANES = 128


def slot_positions(targets, bins):
    onehot = (targets[:, None] == jnp.arange(bins, dtype=jnp.int32)[None, :]).astype(jnp.int32)
    earlier = jnp.cumsum(onehot, axis=0) - onehot
    return jnp.sum(earlier * onehot, axis=1)


def slot_pieces(cap_rows, feat_width):
    tile_rows = 8 * LANES // feat_width if feat_width < 8 * LANES else 1
    whole = [p for p in range(1, cap_rows) if (p * feat_width // LANES) % 8 == 0 and ((cap_rows - p) * feat_width // LANES) % 8 == 0]
    if not whole or cap_rows * feat_width % LANES:
        return (cap_rows,)
    first = min(whole, key=lambda p: abs(2 * p - cap_rows) + (p < cap_rows - p))
    return (first, cap_rows - first)


def wire_of(size, feat_width, experts_all):
    return (experts_all, size * feat_width // LANES, LANES)


def gather_piece(tokens, flat_ids, positions, start, size, experts_all):
    tok_dev = tokens.shape[0]
    inside = (positions >= start) & (positions < start + size)
    slot = jnp.where(inside, flat_ids * size + positions - start, -1).reshape(tok_dev, -1)
    hits = slot[None, :, :] == jnp.arange(experts_all * size, dtype=jnp.int32)[:, None, None]
    onehot = jnp.any(hits, axis=2).astype(tokens.dtype)
    return jnp.dot(onehot, tokens, preferred_element_type=jnp.float32).astype(tokens.dtype)


def combine_piece(rows, weights, flat_ids, positions, start, size):
    tok_dev, picks = weights.shape
    inside = ((positions >= start) & (positions < start + size)).reshape(tok_dev, picks)
    slot = (flat_ids * size + positions - start).reshape(tok_dev, picks)
    hits = slot[:, :, None] == jnp.arange(rows.shape[0], dtype=jnp.int32)[None, None, :]
    dense = jnp.sum(jnp.where(hits & inside[:, :, None], weights[:, :, None], 0.0), axis=1)
    high_part = lax.reduce_precision(dense, exponent_bits=8, mantissa_bits=7)
    high = high_part.astype(jnp.bfloat16)
    low = (dense - high_part).astype(jnp.bfloat16)
    return jnp.dot(high, rows, preferred_element_type=jnp.float32) + jnp.dot(
        low, rows, preferred_element_type=jnp.float32
    )


def expert_rows(flat_rows, w_gate, w_up, w_down):
    gate_part = jnp.dot(flat_rows, w_gate[0], preferred_element_type=jnp.float32)
    up_part = jnp.dot(flat_rows, w_up[0], preferred_element_type=jnp.float32)
    hidden = (jax.nn.silu(gate_part) * up_part).astype(jnp.bfloat16)
    return jnp.dot(hidden, w_down[0], preferred_element_type=jnp.float32).astype(jnp.bfloat16)


def on_device(tokens, group_ids, local_ids, router, w_gate, w_up, w_down):
    tok_dev, feat_width = tokens.shape
    node_size = lax.axis_size("node")
    local_size = lax.axis_size("local")
    experts_all = node_size * local_size
    cap_rows = 5 * tok_dev // (2 * local_size)
    group_count = group_ids.shape[1]
    per_group = local_ids.shape[1] // group_count
    expert_ids = jnp.repeat(group_ids, per_group, axis=1) * local_size + local_ids
    affinity = jax.nn.sigmoid(jnp.dot(tokens, router, preferred_element_type=jnp.float32))
    picked = jnp.take_along_axis(affinity, expert_ids, axis=1)
    picked_total = jnp.sum(picked, axis=1)
    flat_ids = expert_ids.reshape(-1)
    positions = slot_positions(flat_ids, experts_all)
    pieces = slot_pieces(cap_rows, feat_width)
    weights = 2.5 * picked / picked_total[:, None]
    mixed = jnp.zeros((tok_dev, feat_width), jnp.float32)
    starts = [sum(pieces[:i]) for i in range(len(pieces))]
    sent = [
        gather_piece(tokens, flat_ids, positions, start, size, experts_all).reshape(wire_of(size, feat_width, experts_all))
        for start, size in zip(starts, pieces)
    ]
    received = []
    for i, send_rows in enumerate(sent):
        if i:
            received[-1], send_rows = lax.optimization_barrier((received[-1], send_rows))
        received.append(lax.all_to_all(send_rows, ("node", "local"), split_axis=0, concat_axis=0, tiled=True))
    returned = []
    for i, (start, size) in enumerate(zip(starts, pieces)):
        produced = expert_rows(received[i].reshape(-1, feat_width), w_gate, w_up, w_down).reshape(received[i].shape)
        if i:
            returned[-1], produced = lax.optimization_barrier((returned[-1], produced))
        returned.append(lax.all_to_all(produced, ("node", "local"), split_axis=0, concat_axis=0, tiled=True))
    for i, (start, size) in enumerate(zip(starts, pieces)):
        rows = returned[i].reshape(-1, feat_width)
        mixed = mixed + combine_piece(rows, weights, flat_ids, positions, start, size)
    return mixed.astype(jnp.bfloat16)


def solution(mesh):
    return jax.shard_map(
        on_device,
        mesh=mesh,
        in_specs=(
            P(("node", "local"), None),
            P(("node", "local"), None),
            P(("node", "local"), None),
            P(),
            P(("node", "local"), None, None),
            P(("node", "local"), None, None),
            P(("node", "local"), None, None),
        ),
        out_specs=P(("node", "local"), None),
        check_vma=False,
    )
```

```python
import jax
import jax.numpy as jnp
from jax import lax
from jax.sharding import PartitionSpec as P

LANES = 128


def slot_positions(targets, bins):
    onehot = (targets[:, None] == jnp.arange(bins, dtype=jnp.int32)[None, :]).astype(jnp.int32)
    earlier = jnp.cumsum(onehot, axis=0) - onehot
    return jnp.sum(earlier * onehot, axis=1)


def slot_pieces(cap_rows, feat_width):
    tile_rows = 8 * LANES // feat_width if feat_width < 8 * LANES else 1
    whole = [p for p in range(1, cap_rows) if (p * feat_width // LANES) % 8 == 0 and ((cap_rows - p) * feat_width // LANES) % 8 == 0]
    if not whole or cap_rows * feat_width % LANES:
        return (cap_rows,)
    first = min(whole, key=lambda p: abs(2 * p - cap_rows) + (p < cap_rows - p))
    return (first, cap_rows - first)


def wire_of(size, feat_width, experts_all):
    return (experts_all, size * feat_width // LANES, LANES)


def gather_piece(tokens, flat_ids, positions, start, size, experts_all):
    tok_dev = tokens.shape[0]
    inside = (positions >= start) & (positions < start + size)
    slot = jnp.where(inside, flat_ids * size + positions - start, -1).reshape(tok_dev, -1)
    hits = slot[None, :, :] == jnp.arange(experts_all * size, dtype=jnp.int32)[:, None, None]
    onehot = jnp.any(hits, axis=2).astype(tokens.dtype)
    return jnp.dot(onehot, tokens, preferred_element_type=jnp.float32).astype(tokens.dtype)


def gather_piece_wire(tokens, flat_ids, positions, start, size, experts_all):
    tok_dev, feat_width = tokens.shape
    per_row = feat_width // LANES
    inside = (positions >= start) & (positions < start + size)
    slot = jnp.where(inside, flat_ids * size + positions - start, -1).reshape(tok_dev, -1)
    hits = slot[None, :, :] == jnp.arange(experts_all * size, dtype=jnp.int32)[:, None, None]
    owner = jnp.arange(tok_dev, dtype=jnp.int32)[None, :, None]
    source = jnp.max(jnp.where(hits, owner, -1), axis=(1, 2))
    source = jnp.where(source < 0, tok_dev, source)
    padded = jnp.concatenate([tokens, jnp.zeros((1, feat_width), tokens.dtype)], axis=0)
    parts = padded.reshape((tok_dev + 1) * per_row, LANES)
    index = (source[:, None] * per_row + jnp.arange(per_row, dtype=jnp.int32)[None, :]).reshape(-1)
    return parts[index].reshape(wire_of(size, feat_width, experts_all))


def combine_piece(rows, weights, flat_ids, positions, start, size):
    tok_dev, picks = weights.shape
    inside = ((positions >= start) & (positions < start + size)).reshape(tok_dev, picks)
    slot = (flat_ids * size + positions - start).reshape(tok_dev, picks)
    hits = slot[:, :, None] == jnp.arange(rows.shape[0], dtype=jnp.int32)[None, None, :]
    dense = jnp.sum(jnp.where(hits & inside[:, :, None], weights[:, :, None], 0.0), axis=1)
    high_part = lax.reduce_precision(dense, exponent_bits=8, mantissa_bits=7)
    high = high_part.astype(jnp.bfloat16)
    low = (dense - high_part).astype(jnp.bfloat16)
    return jnp.dot(high, rows, preferred_element_type=jnp.float32) + jnp.dot(
        low, rows, preferred_element_type=jnp.float32
    )


def expert_rows(flat_rows, w_gate, w_up, w_down):
    gate_part = jnp.dot(flat_rows, w_gate[0], preferred_element_type=jnp.float32)
    up_part = jnp.dot(flat_rows, w_up[0], preferred_element_type=jnp.float32)
    hidden = (jax.nn.silu(gate_part) * up_part).astype(jnp.bfloat16)
    return jnp.dot(hidden, w_down[0], preferred_element_type=jnp.float32).astype(jnp.bfloat16)


def on_device(tokens, group_ids, local_ids, router, w_gate, w_up, w_down):
    tok_dev, feat_width = tokens.shape
    node_size = lax.axis_size("node")
    local_size = lax.axis_size("local")
    experts_all = node_size * local_size
    cap_rows = 5 * tok_dev // (2 * local_size)
    group_count = group_ids.shape[1]
    per_group = local_ids.shape[1] // group_count
    expert_ids = jnp.repeat(group_ids, per_group, axis=1) * local_size + local_ids
    affinity = jax.nn.sigmoid(jnp.dot(tokens, router, preferred_element_type=jnp.float32))
    picked = jnp.take_along_axis(affinity, expert_ids, axis=1)
    picked_total = jnp.sum(picked, axis=1)
    flat_ids = expert_ids.reshape(-1)
    positions = slot_positions(flat_ids, experts_all)
    pieces = slot_pieces(cap_rows, feat_width)
    weights = 2.5 * picked / picked_total[:, None]
    mixed = jnp.zeros((tok_dev, feat_width), jnp.float32)
    starts = [sum(pieces[:i]) for i in range(len(pieces))]
    sent = [
        gather_piece_wire(tokens, flat_ids, positions, start, size, experts_all)
        if not i
        else gather_piece(tokens, flat_ids, positions, start, size, experts_all).reshape(wire_of(size, feat_width, experts_all))
        for i, (start, size) in enumerate(zip(starts, pieces))
    ]
    received = []
    for i, send_rows in enumerate(sent):
        if i:
            received[-1], send_rows = lax.optimization_barrier((received[-1], send_rows))
        received.append(lax.all_to_all(send_rows, ("node", "local"), split_axis=0, concat_axis=0, tiled=True))
    returned = []
    for i, (start, size) in enumerate(zip(starts, pieces)):
        produced = expert_rows(received[i].reshape(-1, feat_width), w_gate, w_up, w_down).reshape(received[i].shape)
        if i:
            returned[-1], produced = lax.optimization_barrier((returned[-1], produced))
        returned.append(lax.all_to_all(produced, ("node", "local"), split_axis=0, concat_axis=0, tiled=True))
    for i, (start, size) in enumerate(zip(starts, pieces)):
        rows = returned[i].reshape(-1, feat_width)
        mixed = mixed + combine_piece(rows, weights, flat_ids, positions, start, size)
    return mixed.astype(jnp.bfloat16)


def solution(mesh):
    return jax.shard_map(
        on_device,
        mesh=mesh,
        in_specs=(
            P(("node", "local"), None),
            P(("node", "local"), None),
            P(("node", "local"), None),
            P(),
            P(("node", "local"), None, None),
            P(("node", "local"), None, None),
            P(("node", "local"), None, None),
        ),
        out_specs=P(("node", "local"), None),
        check_vma=False,
    )
```

```python
import jax
import jax.numpy as jnp
from jax import lax
from jax.sharding import PartitionSpec as P

LANES = 128


def slot_positions(targets, bins):
    onehot = (targets[:, None] == jnp.arange(bins, dtype=jnp.int32)[None, :]).astype(jnp.int32)
    earlier = jnp.cumsum(onehot, axis=0) - onehot
    return jnp.sum(earlier * onehot, axis=1)


def slot_pieces(cap_rows, feat_width):
    first = cap_rows // 8 * 8
    rest = cap_rows - first
    if first and rest and (rest * feat_width // LANES) % 8 == 0 and feat_width % LANES == 0:
        return (first, rest)
    return (cap_rows,)


def wire_of(size, feat_width, experts_all):
    if size % 8 == 0:
        return (experts_all, size, feat_width)
    return (experts_all, size * feat_width // LANES, LANES)


def gather_piece(tokens, flat_ids, positions, start, size, experts_all):
    tok_dev = tokens.shape[0]
    inside = (positions >= start) & (positions < start + size)
    slot = jnp.where(inside, flat_ids * size + positions - start, -1).reshape(tok_dev, -1)
    hits = slot[None, :, :] == jnp.arange(experts_all * size, dtype=jnp.int32)[:, None, None]
    onehot = jnp.any(hits, axis=2).astype(tokens.dtype)
    return jnp.dot(onehot, tokens, preferred_element_type=jnp.float32).astype(tokens.dtype)


def combine_piece(rows, weights, flat_ids, positions, start, size):
    tok_dev, picks = weights.shape
    inside = ((positions >= start) & (positions < start + size)).reshape(tok_dev, picks)
    slot = (flat_ids * size + positions - start).reshape(tok_dev, picks)
    hits = slot[:, :, None] == jnp.arange(rows.shape[0], dtype=jnp.int32)[None, None, :]
    dense = jnp.sum(jnp.where(hits & inside[:, :, None], weights[:, :, None], 0.0), axis=1)
    high_part = lax.reduce_precision(dense, exponent_bits=8, mantissa_bits=7)
    high = high_part.astype(jnp.bfloat16)
    low = (dense - high_part).astype(jnp.bfloat16)
    return jnp.dot(high, rows, preferred_element_type=jnp.float32) + jnp.dot(
        low, rows, preferred_element_type=jnp.float32
    )


def expert_rows(flat_rows, w_gate, w_up, w_down):
    gate_part = jnp.dot(flat_rows, w_gate[0], preferred_element_type=jnp.float32)
    up_part = jnp.dot(flat_rows, w_up[0], preferred_element_type=jnp.float32)
    hidden = (jax.nn.silu(gate_part) * up_part).astype(jnp.bfloat16)
    return jnp.dot(hidden, w_down[0], preferred_element_type=jnp.float32).astype(jnp.bfloat16)


def on_device(tokens, group_ids, local_ids, router, w_gate, w_up, w_down):
    tok_dev, feat_width = tokens.shape
    node_size = lax.axis_size("node")
    local_size = lax.axis_size("local")
    experts_all = node_size * local_size
    cap_rows = 5 * tok_dev // (2 * local_size)
    group_count = group_ids.shape[1]
    per_group = local_ids.shape[1] // group_count
    expert_ids = jnp.repeat(group_ids, per_group, axis=1) * local_size + local_ids
    affinity = jax.nn.sigmoid(jnp.dot(tokens, router, preferred_element_type=jnp.float32))
    picked = jnp.take_along_axis(affinity, expert_ids, axis=1)
    picked_total = jnp.sum(picked, axis=1)
    flat_ids = expert_ids.reshape(-1)
    positions = slot_positions(flat_ids, experts_all)
    pieces = slot_pieces(cap_rows, feat_width)
    weights = 2.5 * picked / picked_total[:, None]
    mixed = jnp.zeros((tok_dev, feat_width), jnp.float32)
    starts = [sum(pieces[:i]) for i in range(len(pieces))]
    sent = [
        gather_piece(tokens, flat_ids, positions, start, size, experts_all).reshape(wire_of(size, feat_width, experts_all))
        for start, size in zip(starts, pieces)
    ]
    received = []
    for i, send_rows in enumerate(sent):
        if i:
            received[-1], send_rows = lax.optimization_barrier((received[-1], send_rows))
        received.append(lax.all_to_all(send_rows, ("node", "local"), split_axis=0, concat_axis=0, tiled=True))
    returned = []
    for i, (start, size) in enumerate(zip(starts, pieces)):
        produced = expert_rows(received[i].reshape(-1, feat_width), w_gate, w_up, w_down).reshape(received[i].shape)
        if i:
            returned[-1], produced = lax.optimization_barrier((returned[-1], produced))
        returned.append(lax.all_to_all(produced, ("node", "local"), split_axis=0, concat_axis=0, tiled=True))
    for i, (start, size) in enumerate(zip(starts, pieces)):
        rows = returned[i].reshape(-1, feat_width)
        mixed = mixed + combine_piece(rows, weights, flat_ids, positions, start, size)
    return mixed.astype(jnp.bfloat16)


def solution(mesh):
    return jax.shard_map(
        on_device,
        mesh=mesh,
        in_specs=(
            P(("node", "local"), None),
            P(("node", "local"), None),
            P(("node", "local"), None),
            P(),
            P(("node", "local"), None, None),
            P(("node", "local"), None, None),
            P(("node", "local"), None, None),
        ),
        out_specs=P(("node", "local"), None),
        check_vma=False,
    )
```

```python
import jax
import jax.numpy as jnp
from jax import lax
from jax.sharding import PartitionSpec as P

LANES = 128


def slot_positions(targets, bins):
    onehot = (targets[:, None] == jnp.arange(bins, dtype=jnp.int32)[None, :]).astype(jnp.int32)
    earlier = jnp.cumsum(onehot, axis=0) - onehot
    return jnp.sum(earlier * onehot, axis=1)


def slot_pieces(cap_rows, feat_width):
    first = cap_rows // 8 * 8
    rest = cap_rows - first
    if first and rest and (rest * feat_width // LANES) % 8 == 0 and feat_width % LANES == 0:
        return (rest, first)
    return (cap_rows,)


def wire_of(size, feat_width, experts_all):
    if size % 8 == 0:
        return (experts_all, size, feat_width)
    return (experts_all, size * feat_width // LANES, LANES)


def gather_piece(tokens, flat_ids, positions, start, size, experts_all):
    tok_dev = tokens.shape[0]
    inside = (positions >= start) & (positions < start + size)
    slot = jnp.where(inside, flat_ids * size + positions - start, -1).reshape(tok_dev, -1)
    hits = slot[None, :, :] == jnp.arange(experts_all * size, dtype=jnp.int32)[:, None, None]
    onehot = jnp.any(hits, axis=2).astype(tokens.dtype)
    return jnp.dot(onehot, tokens, preferred_element_type=jnp.float32).astype(tokens.dtype)


def combine_piece(rows, weights, flat_ids, positions, start, size):
    tok_dev, picks = weights.shape
    inside = ((positions >= start) & (positions < start + size)).reshape(tok_dev, picks)
    slot = (flat_ids * size + positions - start).reshape(tok_dev, picks)
    hits = slot[:, :, None] == jnp.arange(rows.shape[0], dtype=jnp.int32)[None, None, :]
    dense = jnp.sum(jnp.where(hits & inside[:, :, None], weights[:, :, None], 0.0), axis=1)
    high_part = lax.reduce_precision(dense, exponent_bits=8, mantissa_bits=7)
    high = high_part.astype(jnp.bfloat16)
    low = (dense - high_part).astype(jnp.bfloat16)
    return jnp.dot(high, rows, preferred_element_type=jnp.float32) + jnp.dot(
        low, rows, preferred_element_type=jnp.float32
    )


def expert_rows(flat_rows, w_gate, w_up, w_down):
    gate_part = jnp.dot(flat_rows, w_gate[0], preferred_element_type=jnp.float32)
    up_part = jnp.dot(flat_rows, w_up[0], preferred_element_type=jnp.float32)
    hidden = (jax.nn.silu(gate_part) * up_part).astype(jnp.bfloat16)
    return jnp.dot(hidden, w_down[0], preferred_element_type=jnp.float32).astype(jnp.bfloat16)


def on_device(tokens, group_ids, local_ids, router, w_gate, w_up, w_down):
    tok_dev, feat_width = tokens.shape
    node_size = lax.axis_size("node")
    local_size = lax.axis_size("local")
    experts_all = node_size * local_size
    cap_rows = 5 * tok_dev // (2 * local_size)
    group_count = group_ids.shape[1]
    per_group = local_ids.shape[1] // group_count
    expert_ids = jnp.repeat(group_ids, per_group, axis=1) * local_size + local_ids
    affinity = jax.nn.sigmoid(jnp.dot(tokens, router, preferred_element_type=jnp.float32))
    picked = jnp.take_along_axis(affinity, expert_ids, axis=1)
    picked_total = jnp.sum(picked, axis=1)
    flat_ids = expert_ids.reshape(-1)
    positions = slot_positions(flat_ids, experts_all)
    pieces = slot_pieces(cap_rows, feat_width)
    weights = 2.5 * picked / picked_total[:, None]
    mixed = jnp.zeros((tok_dev, feat_width), jnp.float32)
    starts = [sum(pieces[:i]) for i in range(len(pieces))]
    sent = [
        gather_piece(tokens, flat_ids, positions, start, size, experts_all).reshape(wire_of(size, feat_width, experts_all))
        for start, size in zip(starts, pieces)
    ]
    received = []
    for i, send_rows in enumerate(sent):
        if i:
            received[-1], send_rows = lax.optimization_barrier((received[-1], send_rows))
        received.append(lax.all_to_all(send_rows, ("node", "local"), split_axis=0, concat_axis=0, tiled=True))
    returned = []
    for i, (start, size) in enumerate(zip(starts, pieces)):
        produced = expert_rows(received[i].reshape(-1, feat_width), w_gate, w_up, w_down).reshape(received[i].shape)
        if i:
            returned[-1], produced = lax.optimization_barrier((returned[-1], produced))
        returned.append(lax.all_to_all(produced, ("node", "local"), split_axis=0, concat_axis=0, tiled=True))
    for i, (start, size) in enumerate(zip(starts, pieces)):
        rows = returned[i].reshape(-1, feat_width)
        mixed = mixed + combine_piece(rows, weights, flat_ids, positions, start, size)
    return mixed.astype(jnp.bfloat16)


def solution(mesh):
    return jax.shard_map(
        on_device,
        mesh=mesh,
        in_specs=(
            P(("node", "local"), None),
            P(("node", "local"), None),
            P(("node", "local"), None),
            P(),
            P(("node", "local"), None, None),
            P(("node", "local"), None, None),
            P(("node", "local"), None, None),
        ),
        out_specs=P(("node", "local"), None),
        check_vma=False,
    )
```

```python
import jax
import jax.numpy as jnp
from jax import lax
from jax.sharding import PartitionSpec as P

LANES = 128


def slot_positions(targets, bins):
    onehot = (targets[:, None] == jnp.arange(bins, dtype=jnp.int32)[None, :]).astype(jnp.int32)
    earlier = jnp.cumsum(onehot, axis=0) - onehot
    return jnp.sum(earlier * onehot, axis=1)


def slot_pieces(cap_rows, feat_width):
    first = cap_rows // 8 * 8
    rest = cap_rows - first
    if first and rest and (rest * feat_width // LANES) % 8 == 0 and feat_width % LANES == 0:
        return (rest, first)
    return (cap_rows,)


def wire_of(size, feat_width, experts_all):
    if size % 8 == 0:
        return (experts_all, size, feat_width)
    return (experts_all, size * feat_width // LANES, LANES)


def gather_piece(tokens, flat_ids, positions, start, size, experts_all):
    tok_dev = tokens.shape[0]
    inside = (positions >= start) & (positions < start + size)
    slot = jnp.where(inside, flat_ids * size + positions - start, -1).reshape(tok_dev, -1)
    hits = slot[None, :, :] == jnp.arange(experts_all * size, dtype=jnp.int32)[:, None, None]
    onehot = jnp.any(hits, axis=2).astype(tokens.dtype)
    return jnp.dot(onehot, tokens, preferred_element_type=jnp.float32).astype(tokens.dtype)


def combine_piece(rows, weights, flat_ids, positions, start, size):
    tok_dev, picks = weights.shape
    inside = ((positions >= start) & (positions < start + size)).reshape(tok_dev, picks)
    slot = (flat_ids * size + positions - start).reshape(tok_dev, picks)
    hits = slot[:, :, None] == jnp.arange(rows.shape[0], dtype=jnp.int32)[None, None, :]
    dense = jnp.sum(jnp.where(hits & inside[:, :, None], weights[:, :, None], 0.0), axis=1)
    high_part = lax.reduce_precision(dense, exponent_bits=8, mantissa_bits=7)
    high = high_part.astype(jnp.bfloat16)
    low = (dense - high_part).astype(jnp.bfloat16)
    both = jnp.dot(jnp.concatenate([high, low], axis=0), rows, preferred_element_type=jnp.float32)
    return both[:tok_dev] + both[tok_dev:]


def expert_rows(flat_rows, w_gate, w_up, w_down):
    gate_part = jnp.dot(flat_rows, w_gate[0], preferred_element_type=jnp.float32)
    up_part = jnp.dot(flat_rows, w_up[0], preferred_element_type=jnp.float32)
    hidden = (jax.nn.silu(gate_part) * up_part).astype(jnp.bfloat16)
    return jnp.dot(hidden, w_down[0], preferred_element_type=jnp.float32).astype(jnp.bfloat16)


def on_device(tokens, group_ids, local_ids, router, w_gate, w_up, w_down):
    tok_dev, feat_width = tokens.shape
    node_size = lax.axis_size("node")
    local_size = lax.axis_size("local")
    experts_all = node_size * local_size
    cap_rows = 5 * tok_dev // (2 * local_size)
    group_count = group_ids.shape[1]
    per_group = local_ids.shape[1] // group_count
    expert_ids = jnp.repeat(group_ids, per_group, axis=1) * local_size + local_ids
    affinity = jax.nn.sigmoid(jnp.dot(tokens, router, preferred_element_type=jnp.float32))
    picked = jnp.take_along_axis(affinity, expert_ids, axis=1)
    picked_total = jnp.sum(picked, axis=1)
    flat_ids = expert_ids.reshape(-1)
    positions = slot_positions(flat_ids, experts_all)
    pieces = slot_pieces(cap_rows, feat_width)
    weights = 2.5 * picked / picked_total[:, None]
    mixed = jnp.zeros((tok_dev, feat_width), jnp.float32)
    starts = [sum(pieces[:i]) for i in range(len(pieces))]
    sent = [
        gather_piece(tokens, flat_ids, positions, start, size, experts_all).reshape(wire_of(size, feat_width, experts_all))
        for start, size in zip(starts, pieces)
    ]
    received = []
    for i, send_rows in enumerate(sent):
        if i:
            received[-1], send_rows = lax.optimization_barrier((received[-1], send_rows))
        received.append(lax.all_to_all(send_rows, ("node", "local"), split_axis=0, concat_axis=0, tiled=True))
    returned = []
    for i, (start, size) in enumerate(zip(starts, pieces)):
        produced = expert_rows(received[i].reshape(-1, feat_width), w_gate, w_up, w_down).reshape(received[i].shape)
        if i:
            returned[-1], produced = lax.optimization_barrier((returned[-1], produced))
        returned.append(lax.all_to_all(produced, ("node", "local"), split_axis=0, concat_axis=0, tiled=True))
    for i, (start, size) in enumerate(zip(starts, pieces)):
        rows = returned[i].reshape(-1, feat_width)
        mixed = mixed + combine_piece(rows, weights, flat_ids, positions, start, size)
    return mixed.astype(jnp.bfloat16)


def solution(mesh):
    return jax.shard_map(
        on_device,
        mesh=mesh,
        in_specs=(
            P(("node", "local"), None),
            P(("node", "local"), None),
            P(("node", "local"), None),
            P(),
            P(("node", "local"), None, None),
            P(("node", "local"), None, None),
            P(("node", "local"), None, None),
        ),
        out_specs=P(("node", "local"), None),
        check_vma=False,
    )
```

```python
import jax
import jax.numpy as jnp
from jax import lax
from jax.sharding import PartitionSpec as P

LANES = 128


def slot_positions(targets, bins):
    onehot = (targets[:, None] == jnp.arange(bins, dtype=jnp.int32)[None, :]).astype(jnp.int32)
    earlier = jnp.cumsum(onehot, axis=0) - onehot
    return jnp.sum(earlier * onehot, axis=1)


def slot_pieces(cap_rows, feat_width):
    first = cap_rows // 8 * 8
    rest = cap_rows - first
    if first and rest and (rest * feat_width // LANES) % 8 == 0 and feat_width % LANES == 0:
        return (rest, first)
    return (cap_rows,)


def wire_of(size, feat_width, experts_all):
    if size % 8 == 0:
        return (experts_all, size, feat_width)
    return (experts_all, size * feat_width // LANES, LANES)


def gather_piece(tokens, flat_ids, positions, start, size, experts_all):
    tok_dev = tokens.shape[0]
    inside = (positions >= start) & (positions < start + size)
    slot = jnp.where(inside, flat_ids * size + positions - start, -1).reshape(tok_dev, -1)
    hits = slot[None, :, :] == jnp.arange(experts_all * size, dtype=jnp.int32)[:, None, None]
    onehot = jnp.any(hits, axis=2).astype(tokens.dtype)
    return jnp.dot(onehot, tokens, preferred_element_type=jnp.float32).astype(tokens.dtype)


def combine_piece(rows, weights, flat_ids, positions, start, size):
    tok_dev, picks = weights.shape
    inside = ((positions >= start) & (positions < start + size)).reshape(tok_dev, picks)
    slot = (flat_ids * size + positions - start).reshape(tok_dev, picks)
    hits = slot[:, :, None] == jnp.arange(rows.shape[0], dtype=jnp.int32)[None, None, :]
    dense = jnp.sum(jnp.where(hits & inside[:, :, None], weights[:, :, None], 0.0), axis=1)
    high_part = lax.reduce_precision(dense, exponent_bits=8, mantissa_bits=7)
    high = high_part.astype(jnp.bfloat16)
    low = (dense - high_part).astype(jnp.bfloat16)
    both = jnp.dot(jnp.concatenate([high, low], axis=0), rows, preferred_element_type=jnp.float32)
    return both[:tok_dev] + both[tok_dev:]


def expert_rows(flat_rows, w_gate_up, w_down):
    both = jnp.dot(flat_rows, w_gate_up, preferred_element_type=jnp.float32)
    ff = w_down.shape[1]
    gate_part, up_part = both[:, :ff], both[:, ff:]
    hidden = (jax.nn.silu(gate_part) * up_part).astype(jnp.bfloat16)
    return jnp.dot(hidden, w_down[0], preferred_element_type=jnp.float32).astype(jnp.bfloat16)


def on_device(tokens, group_ids, local_ids, router, w_gate, w_up, w_down):
    tok_dev, feat_width = tokens.shape
    node_size = lax.axis_size("node")
    local_size = lax.axis_size("local")
    experts_all = node_size * local_size
    cap_rows = 5 * tok_dev // (2 * local_size)
    group_count = group_ids.shape[1]
    per_group = local_ids.shape[1] // group_count
    expert_ids = jnp.repeat(group_ids, per_group, axis=1) * local_size + local_ids
    affinity = jax.nn.sigmoid(jnp.dot(tokens, router, preferred_element_type=jnp.float32))
    picked = jnp.take_along_axis(affinity, expert_ids, axis=1)
    picked_total = jnp.sum(picked, axis=1)
    flat_ids = expert_ids.reshape(-1)
    positions = slot_positions(flat_ids, experts_all)
    pieces = slot_pieces(cap_rows, feat_width)
    weights = 2.5 * picked / picked_total[:, None]
    mixed = jnp.zeros((tok_dev, feat_width), jnp.float32)
    w_gate_up = jnp.concatenate([w_gate[0], w_up[0]], axis=1)
    starts = [sum(pieces[:i]) for i in range(len(pieces))]
    sent = [
        gather_piece(tokens, flat_ids, positions, start, size, experts_all).reshape(wire_of(size, feat_width, experts_all))
        for start, size in zip(starts, pieces)
    ]
    received = []
    for i, send_rows in enumerate(sent):
        if i:
            received[-1], send_rows = lax.optimization_barrier((received[-1], send_rows))
        received.append(lax.all_to_all(send_rows, ("node", "local"), split_axis=0, concat_axis=0, tiled=True))
    returned = []
    for i, (start, size) in enumerate(zip(starts, pieces)):
        produced = expert_rows(received[i].reshape(-1, feat_width), w_gate_up, w_down).reshape(received[i].shape)
        if i:
            returned[-1], produced = lax.optimization_barrier((returned[-1], produced))
        returned.append(lax.all_to_all(produced, ("node", "local"), split_axis=0, concat_axis=0, tiled=True))
    for i, (start, size) in enumerate(zip(starts, pieces)):
        rows = returned[i].reshape(-1, feat_width)
        mixed = mixed + combine_piece(rows, weights, flat_ids, positions, start, size)
    return mixed.astype(jnp.bfloat16)


def solution(mesh):
    return jax.shard_map(
        on_device,
        mesh=mesh,
        in_specs=(
            P(("node", "local"), None),
            P(("node", "local"), None),
            P(("node", "local"), None),
            P(),
            P(("node", "local"), None, None),
            P(("node", "local"), None, None),
            P(("node", "local"), None, None),
        ),
        out_specs=P(("node", "local"), None),
        check_vma=False,
    )
```

```python
import jax
import jax.numpy as jnp
from jax import lax
from jax.sharding import PartitionSpec as P

LANES = 128


def slot_positions(targets, bins):
    onehot = (targets[:, None] == jnp.arange(bins, dtype=jnp.int32)[None, :]).astype(jnp.int32)
    earlier = jnp.cumsum(onehot, axis=0) - onehot
    return jnp.sum(earlier * onehot, axis=1)


def slot_pieces(cap_rows, feat_width):
    first = cap_rows // 8 * 8
    rest = cap_rows - first
    if first and rest and (rest * feat_width // LANES) % 8 == 0 and feat_width % LANES == 0:
        return (rest, first)
    return (cap_rows,)


def wire_of(size, feat_width, experts_all):
    if size % 8 == 0:
        return (experts_all, size, feat_width)
    return (experts_all, size * feat_width // LANES, LANES)


def gather_piece(tokens, flat_ids, positions, start, size, experts_all):
    tok_dev = tokens.shape[0]
    inside = (positions >= start) & (positions < start + size)
    slot = jnp.where(inside, flat_ids * size + positions - start, -1).reshape(tok_dev, -1)
    hits = slot[None, :, :] == jnp.arange(experts_all * size, dtype=jnp.int32)[:, None, None]
    onehot = jnp.any(hits, axis=2).astype(tokens.dtype)
    return jnp.dot(onehot, tokens, preferred_element_type=jnp.float32).astype(tokens.dtype)


def combine_piece(rows, weights, flat_ids, positions, start, size):
    tok_dev, picks = weights.shape
    inside = ((positions >= start) & (positions < start + size)).reshape(tok_dev, picks)
    slot = (flat_ids * size + positions - start).reshape(tok_dev, picks)
    hits = slot[:, :, None] == jnp.arange(rows.shape[0], dtype=jnp.int32)[None, None, :]
    dense = jnp.sum(jnp.where(hits & inside[:, :, None], weights[:, :, None], 0.0), axis=1)
    high_part = lax.reduce_precision(dense, exponent_bits=8, mantissa_bits=7)
    high = high_part.astype(jnp.bfloat16)
    low = (dense - high_part).astype(jnp.bfloat16)
    stacked = jnp.concatenate([high, low], axis=1)
    return jnp.dot(stacked, jnp.concatenate([rows, rows], axis=0), preferred_element_type=jnp.float32)


def expert_rows(flat_rows, w_gate, w_up, w_down):
    gate_part = jnp.dot(flat_rows, w_gate[0], preferred_element_type=jnp.float32)
    up_part = jnp.dot(flat_rows, w_up[0], preferred_element_type=jnp.float32)
    hidden = (jax.nn.silu(gate_part) * up_part).astype(jnp.bfloat16)
    return jnp.dot(hidden, w_down[0], preferred_element_type=jnp.float32).astype(jnp.bfloat16)


def on_device(tokens, group_ids, local_ids, router, w_gate, w_up, w_down):
    tok_dev, feat_width = tokens.shape
    node_size = lax.axis_size("node")
    local_size = lax.axis_size("local")
    experts_all = node_size * local_size
    cap_rows = 5 * tok_dev // (2 * local_size)
    group_count = group_ids.shape[1]
    per_group = local_ids.shape[1] // group_count
    expert_ids = jnp.repeat(group_ids, per_group, axis=1) * local_size + local_ids
    affinity = jax.nn.sigmoid(jnp.dot(tokens, router, preferred_element_type=jnp.float32))
    picked = jnp.take_along_axis(affinity, expert_ids, axis=1)
    picked_total = jnp.sum(picked, axis=1)
    flat_ids = expert_ids.reshape(-1)
    positions = slot_positions(flat_ids, experts_all)
    pieces = slot_pieces(cap_rows, feat_width)
    weights = 2.5 * picked / picked_total[:, None]
    mixed = jnp.zeros((tok_dev, feat_width), jnp.float32)
    starts = [sum(pieces[:i]) for i in range(len(pieces))]
    sent = [
        gather_piece(tokens, flat_ids, positions, start, size, experts_all).reshape(wire_of(size, feat_width, experts_all))
        for start, size in zip(starts, pieces)
    ]
    received = []
    for i, send_rows in enumerate(sent):
        if i:
            received[-1], send_rows = lax.optimization_barrier((received[-1], send_rows))
        received.append(lax.all_to_all(send_rows, ("node", "local"), split_axis=0, concat_axis=0, tiled=True))
    returned = []
    for i, (start, size) in enumerate(zip(starts, pieces)):
        produced = expert_rows(received[i].reshape(-1, feat_width), w_gate, w_up, w_down).reshape(received[i].shape)
        if i:
            returned[-1], produced = lax.optimization_barrier((returned[-1], produced))
        returned.append(lax.all_to_all(produced, ("node", "local"), split_axis=0, concat_axis=0, tiled=True))
    for i, (start, size) in enumerate(zip(starts, pieces)):
        rows = returned[i].reshape(-1, feat_width)
        mixed = mixed + combine_piece(rows, weights, flat_ids, positions, start, size)
    return mixed.astype(jnp.bfloat16)


def solution(mesh):
    return jax.shard_map(
        on_device,
        mesh=mesh,
        in_specs=(
            P(("node", "local"), None),
            P(("node", "local"), None),
            P(("node", "local"), None),
            P(),
            P(("node", "local"), None, None),
            P(("node", "local"), None, None),
            P(("node", "local"), None, None),
        ),
        out_specs=P(("node", "local"), None),
        check_vma=False,
    )
```

```python
import jax
import jax.numpy as jnp
from jax import lax
from jax.sharding import PartitionSpec as P

LANES = 128


def slot_positions(targets, bins):
    onehot = (targets[:, None] == jnp.arange(bins, dtype=jnp.int32)[None, :]).astype(jnp.int32)
    earlier = jnp.cumsum(onehot, axis=0) - onehot
    return jnp.sum(earlier * onehot, axis=1)


def slot_pieces(cap_rows, feat_width):
    first = cap_rows // 8 * 8
    rest = cap_rows - first
    if first and rest and (rest * feat_width // LANES) % 8 == 0 and feat_width % LANES == 0:
        return (rest, first)
    return (cap_rows,)


def wire_of(size, feat_width, experts_all):
    if size % 8 == 0:
        return (experts_all, size, feat_width)
    return (experts_all, size * feat_width // LANES, LANES)


def gather_piece(tokens, flat_ids, positions, start, size, experts_all):
    tok_dev = tokens.shape[0]
    inside = (positions >= start) & (positions < start + size)
    slot = jnp.where(inside, flat_ids * size + positions - start, -1).reshape(tok_dev, -1)
    hits = slot[None, :, :] == jnp.arange(experts_all * size, dtype=jnp.int32)[:, None, None]
    onehot = jnp.any(hits, axis=2).astype(tokens.dtype)
    return jnp.dot(onehot, tokens, preferred_element_type=jnp.float32).astype(tokens.dtype)


def combine_piece(rows, weights, flat_ids, positions, start, size):
    tok_dev, picks = weights.shape
    inside = ((positions >= start) & (positions < start + size)).reshape(tok_dev, picks)
    slot = (flat_ids * size + positions - start).reshape(tok_dev, picks)
    hits = slot[:, :, None] == jnp.arange(rows.shape[0], dtype=jnp.int32)[None, None, :]
    dense = jnp.sum(jnp.where(hits & inside[:, :, None], weights[:, :, None], 0.0), axis=1)
    high_part = lax.reduce_precision(dense, exponent_bits=8, mantissa_bits=7)
    high = high_part.astype(jnp.bfloat16)
    low = (dense - high_part).astype(jnp.bfloat16)
    both = jnp.dot(jnp.concatenate([high, low], axis=0), rows, preferred_element_type=jnp.float32)
    return both[:tok_dev] + both[tok_dev:]


def expert_rows(flat_rows, w_gate, w_up, w_down):
    gate_part = jnp.dot(flat_rows, w_gate[0], preferred_element_type=jnp.float32)
    up_part = jnp.dot(flat_rows, w_up[0], preferred_element_type=jnp.float32)
    hidden = (jax.nn.silu(gate_part) * up_part).astype(jnp.bfloat16)
    return jnp.dot(hidden, w_down[0], preferred_element_type=jnp.float32).astype(jnp.bfloat16)


def on_device(tokens, group_ids, local_ids, router, w_gate, w_up, w_down):
    tok_dev, feat_width = tokens.shape
    node_size = lax.axis_size("node")
    local_size = lax.axis_size("local")
    experts_all = node_size * local_size
    cap_rows = 5 * tok_dev // (2 * local_size)
    group_count = group_ids.shape[1]
    per_group = local_ids.shape[1] // group_count
    expert_ids = jnp.repeat(group_ids, per_group, axis=1) * local_size + local_ids
    affinity = jax.nn.sigmoid(jnp.dot(tokens, router, preferred_element_type=jnp.float32))
    picked = jnp.take_along_axis(affinity, expert_ids, axis=1)
    picked_total = jnp.sum(picked, axis=1)
    flat_ids = expert_ids.reshape(-1)
    positions = slot_positions(flat_ids, experts_all)
    pieces = slot_pieces(cap_rows, feat_width)
    weights = 2.5 * picked / picked_total[:, None]
    mixed = jnp.zeros((tok_dev, feat_width), jnp.float32)
    starts = [sum(pieces[:i]) for i in range(len(pieces))]
    sent = [
        gather_piece(tokens, flat_ids, positions, start, size, experts_all).reshape(wire_of(size, feat_width, experts_all))
        for start, size in zip(starts, pieces)
    ]
    received = []
    for i, send_rows in enumerate(sent):
        if i:
            received[-1], send_rows = lax.optimization_barrier((received[-1], send_rows))
        received.append(lax.all_to_all(send_rows, ("node", "local"), split_axis=0, concat_axis=0, tiled=True))
    returned = []
    for i, (start, size) in enumerate(zip(starts, pieces)):
        produced = expert_rows(received[i].reshape(-1, feat_width), w_gate, w_up, w_down).reshape(received[i].shape)
        returned.append(lax.all_to_all(produced, ("node", "local"), split_axis=0, concat_axis=0, tiled=True))
    for i, (start, size) in enumerate(zip(starts, pieces)):
        rows = returned[i].reshape(-1, feat_width)
        mixed = mixed + combine_piece(rows, weights, flat_ids, positions, start, size)
    return mixed.astype(jnp.bfloat16)


def solution(mesh):
    return jax.shard_map(
        on_device,
        mesh=mesh,
        in_specs=(
            P(("node", "local"), None),
            P(("node", "local"), None),
            P(("node", "local"), None),
            P(),
            P(("node", "local"), None, None),
            P(("node", "local"), None, None),
            P(("node", "local"), None, None),
        ),
        out_specs=P(("node", "local"), None),
        check_vma=False,
    )
```
